256 devices in a mesh: dp: 4 (over z_lo, core), expert: 64 (over x, y, z_hi).
Axes of the slice: x: 4, y: 4, z: 8 (z_hi: 4, z_lo: 2; z = z_hi * 2 + z_lo), core: 2. Of those that a mesh axis runs over, the one named last changes fastest.
Arguments:
- tokens: bfloat16 [8192, 3584], P('expert'), may hold values from -6 to 6
- cotangent: bfloat16 [8192, 3584], P('expert'), may hold values from -0.29882812 to 0.29882812
- probs: bfloat16 [8192, 8], P('expert'), may hold values from 0.049804688 to 0.59765625
- expert_ids: int32 [8192, 8], P('expert'), may hold values from 0 to 63, all different within a row; in each aligned block of 128 rows (0 to 127, 128 to 255, ...) at most 18 rows name the same one
- w_in: bfloat16 [64, 3584, 1024], P('expert', None, 'dp'), may hold values from -0.1875 to 0.1875
- w_out: bfloat16 [64, 1024, 3584], P('expert', 'dp'), may hold values from -0.1875 to 0.1875
Outputs:
- grad_tokens: bfloat16 [8192, 3584], P('expert')
- gate_grad: bfloat16 [8192, 8], P('expert')
- grad_w_in: bfloat16 [64, 3584, 1024], P('expert', None, 'dp')
- grad_w_out: bfloat16 [64, 1024, 3584], P('expert', 'dp')
The draws below stay inside these ranges and needn't reach their ends.
Inputs may be any that keep to these rules, and one draw needn't show every extreme that they name: `expert_ids`: each row names 8 different experts. In each aligned block of 128 rows (the tokens of one index of expert) no expert is named by more than 18 rows, a bound that some block reaches.
All inputs are finite; a program needn't handle non-finite values.
Results may differ from the reference program's by a relative error of at most 0.0064.
Values may be sent and summed in bfloat16 or wider, within the bound.
No kernel may reach another device: no remote copies, remote signals or barrier semaphores. Data moves between devices by JAX's collectives and lax.ppermute only.
A program may use at most 192 MiB of HBM per device.

```python
import math
import jax
import jax.numpy as jnp
import numpy as np
from jax import lax

D = 3584
FF = 1024
TOP = 8
TOK_DEV = 128
EXPERTS = 64
FF_DEV = 256
CAP = 18
TOKENS = 8192
N_DP = 4


def level_of(own_key, extent, shards, smallest, high):
    factor_of, own = 1.0, jax.random.fold_in(own_key, 6)
    for position, blocks in shards:
        draws = jnp.exp(jax.random.uniform(jax.random.fold_in(own, position), (blocks,), jnp.float32, smallest / len(shards), high / len(shards)))
        factor_of = factor_of * jnp.repeat(draws, extent[position] // blocks).reshape([-1 if axis == position else 1 for axis in range(len(extent))])
    return factor_of


def shared_out(stream_key, own, number, rows, count, top, limit, lean):
    sequence = jax.random.permutation(stream_key, count)
    heavy_load, common = portions_of(count, rows * top, limit, lean, True), portions_of(count, rows * top, limit, lean, False)
    places = jnp.arange(count)

    def named(tallies, rotation):
        used = int((tallies > 0).sum())
        fixed = max(1, used // 4)
        shifted = fixed + (places - fixed + rotation * (used - fixed)) % max(1, count - fixed)
        return jnp.zeros((count,), jnp.int32).at[sequence[jnp.where(places < fixed, places, shifted)]].set(jnp.asarray(tallies, jnp.int32))

    tallies = jnp.where(number % 4 == 0, named(heavy_load, number // 4), named(common, number - number // 4 - 1))
    mixed = jax.random.permutation(jax.random.fold_in(own, 3), count)
    source_of, sink = mixed[0:count // 2 * 2:2], mixed[1:count // 2 * 2:2]
    margin = jnp.minimum(tallies[source_of] - 1, limit - tallies[sink]) // 2
    margin = jnp.where((source_of == sequence[0]) | (sink == sequence[0]) | (tallies[sink] == 0), 0, jnp.maximum(margin, 0))
    shifted = jax.random.randint(jax.random.fold_in(own, 4), (count // 2,), 0, 1 << 20) % (margin + 1)
    tallies = tallies.at[source_of].add(-shifted).at[sink].add(shifted)
    members = jnp.searchsorted(jnp.cumsum(tallies), jnp.arange(rows * top), side="right").astype(jnp.int32)
    listing = members.reshape(top, rows).T
    listing = listing[jax.random.permutation(jax.random.fold_in(own, 1), rows)]
    rotation = jax.random.randint(jax.random.fold_in(own, 2), (rows, 1), 0, top)
    return jnp.take_along_axis(listing, (jnp.arange(top)[None, :] + rotation) % top, axis=1)


def portions_of(count, total, bound, skew, full):
    weights = [(1 << 20) // math.isqrt(rank ** skew) + 1 for rank in range(1, count + 1)]
    largest = bound if full else min(bound, max(-(-total // count), total * weights[0] // sum(weights)))
    least = 1 if total - largest >= count - 1 else 0
    counts, surplus = [largest] + [least] * (count - 1), total - largest - least * (count - 1)
    while surplus > 0:
        candidates = [i for i in range(1, count) if counts[i] < largest] or [i for i in range(1, count) if counts[i] < bound]
        whole, budget = sum([weights[i] for i in candidates]), surplus
        for i in candidates:
            addition = min(bound - counts[i], max(1, budget * weights[i] // whole), surplus)
            counts[i] = counts[i] + addition
            surplus = surplus - addition
    return np.array(counts)


def noise(rng, dims, width, most, pieces=(), kind=jnp.bfloat16):
    array = jax.random.normal(rng, dims, jnp.float32) * width
    if len(pieces) > 0:
        array = level_of(rng, dims, pieces, -0.22, 0.18) * array
    return jnp.clip(array, min=-most, max=most).astype(kind)


def setup_inputs(seed: int = 0) -> dict:
    key_of = jax.random.split(jax.random.key(seed), 7)
    tokens = noise(key_of[0], (TOKENS, D), 1.0, 6.0, ((0, 64),))
    cotangent = noise(key_of[1], (TOKENS, D), 0.05, 0.29882812, ((0, 64),))
    probs = jnp.clip(0.049804688 + 0.54785156 * jax.random.uniform(key_of[2], (TOKENS, TOP), jnp.float32) ** level_of(key_of[2], (TOKENS, TOP), ((0, 64),), -0.2, 0.2), 0.049804688, 0.59765625).astype(jnp.bfloat16)
    expert_ids_keys = jax.random.split(jax.random.fold_in(key_of[3], 1), TOKENS // TOK_DEV)
    expert_ids_turns = jax.random.permutation(jax.random.fold_in(key_of[3], 3), TOKENS // TOK_DEV)
    expert_ids = jax.vmap(lambda own, number: shared_out(jax.random.fold_in(key_of[3], 2), own, number, TOK_DEV, EXPERTS, TOP, CAP, 2))(expert_ids_keys, expert_ids_turns).reshape((TOKENS, TOP))
    w_in = noise(key_of[4], (EXPERTS, D, FF), (D // 4) ** -0.5, 0.1875, ((0, 64), (2, 4)))
    w_out = noise(key_of[5], (EXPERTS, FF, D), FF ** -0.5, 0.1875, ((0, 64), (1, 4)))
    return dict(tokens=tokens, cotangent=cotangent, probs=probs, expert_ids=expert_ids, w_in=w_in, w_out=w_out)


def block_terms(rows_x, rows_u, rows_p, block_in, block_out):
    hidden = jnp.dot(rows_x, block_in, preferred_element_type=jnp.float32)
    act = jax.nn.silu(hidden).astype(jnp.bfloat16)
    output = jnp.dot(act, block_out, preferred_element_type=jnp.float32)
    score = jnp.sum(output * rows_u.astype(jnp.float32), axis=1)
    scaled = (rows_p.astype(jnp.float32)[:, None] * rows_u.astype(jnp.float32)).astype(jnp.bfloat16)
    back = lax.dot_general(scaled, block_out, (((1,), (1,)), ((), ())), preferred_element_type=jnp.float32)
    sigma = jax.nn.sigmoid(hidden)
    inner = (sigma * (1.0 + hidden * (1.0 - sigma)) * back).astype(jnp.bfloat16)
    grad_out = lax.dot_general(act, scaled, (((0,), (0,)), ((), ())), preferred_element_type=jnp.float32)
    grad_in = lax.dot_general(rows_x, inner, (((0,), (0,)), ((), ())), preferred_element_type=jnp.float32)
    row_grad = lax.dot_general(inner, block_in, (((1,), (1,)), ((), ())), preferred_element_type=jnp.float32)
    return row_grad, score, grad_in, grad_out


def reference(tokens, cotangent, probs, expert_ids, w_in, w_out):
    blocks = TOKENS // TOK_DEV
    flat = expert_ids.reshape(blocks, TOK_DEV * TOP)
    onehot = (flat[:, :, None] == jnp.arange(EXPERTS, dtype=jnp.int32)[None, None, :]).astype(jnp.int32)
    slot = jnp.sum((jnp.cumsum(onehot, axis=1) - onehot) * onehot, axis=2).astype(jnp.int32)
    global_slot = jnp.arange(blocks, dtype=jnp.int32)[:, None] * CAP + slot
    pairs = jnp.arange(TOKENS * TOP, dtype=jnp.int32)
    table = jnp.full((EXPERTS, blocks * CAP), -1, dtype=jnp.int32)
    table = table.at[flat.reshape(-1), global_slot.reshape(-1)].set(pairs)
    probs_flat = probs.reshape(-1)

    def one_expert(carry, inputs):
        grad_x, grad_gate = carry
        row_ids, weight_in, weight_out = inputs
        live = row_ids >= 0
        pair_id = jnp.where(live, row_ids, 0).astype(jnp.int32)
        token_id = (pair_id // TOP).astype(jnp.int32)
        keep = live.astype(jnp.bfloat16)
        rows_x = tokens[token_id] * keep[:, None]
        rows_u = cotangent[token_id] * keep[:, None]
        rows_p = probs_flat[pair_id] * keep
        row_total = jnp.zeros((rows_x.shape[0], D), jnp.float32)
        score_total = jnp.zeros((rows_x.shape[0],), jnp.float32)
        grads_in = []
        grads_out = []
        for part in range(N_DP):
            start = part * FF_DEV
            row_grad, score, grad_in, grad_out = block_terms(
                rows_x, rows_u, rows_p, weight_in[:, start:start + FF_DEV], weight_out[start:start + FF_DEV, :])
            row_total = row_total + lax.optimization_barrier(row_grad.astype(jnp.bfloat16)).astype(jnp.float32)
            score_total = score_total + lax.optimization_barrier(score.astype(jnp.bfloat16)).astype(jnp.float32)
            grads_in.append(grad_in)
            grads_out.append(grad_out)
        grad_x = grad_x.at[token_id].add(jnp.where(live[:, None], row_total, jnp.float32(0.0)))
        grad_gate = grad_gate.at[pair_id].add(jnp.where(live, score_total, jnp.float32(0.0)))
        whole_in = jnp.concatenate(grads_in, axis=1).astype(jnp.bfloat16)
        whole_out = jnp.concatenate(grads_out, axis=0).astype(jnp.bfloat16)
        return (grad_x, grad_gate), (whole_in, whole_out)

    start_carry = (jnp.zeros((TOKENS, D), jnp.float32), jnp.zeros((TOKENS * TOP,), jnp.float32))
    (grad_x, grad_gate), (grad_w_in, grad_w_out) = lax.scan(one_expert, start_carry, (table, w_in, w_out))
    return (grad_x.astype(jnp.bfloat16), grad_gate.reshape(TOKENS, TOP).astype(jnp.bfloat16), grad_w_in, grad_w_out)
```

```python
import jax
import jax.numpy as jnp
from jax import lax
from jax.sharding import PartitionSpec as P


def slot_tables(expert_ids, capacity, experts):
    count, top = expert_ids.shape
    flat = expert_ids.reshape(count * top)
    onehot = (flat[:, None] == jnp.arange(experts, dtype=jnp.int32)[None, :]).astype(jnp.int32)
    slot = jnp.sum((jnp.cumsum(onehot, axis=0) - onehot) * onehot, axis=1)
    target = flat * capacity + slot
    placing = (target[:, None] == jnp.arange(experts * capacity, dtype=jnp.int32)[None, :]).astype(
        jnp.float32
    )
    picker = jnp.sum(placing.reshape(count, top, experts * capacity), axis=1)
    return (target, placing, picker)


def expert_terms(all_x, all_u, rows_p, block_in, block_out):
    quarters, rows, part = all_x.shape
    ff = block_in.shape[1]
    w_in_q = block_in.reshape(quarters, part, ff)
    w_out_q = block_out.reshape(ff, quarters, part)
    hidden = jnp.einsum("qrc,qcf->rf", all_x, w_in_q, preferred_element_type=jnp.float32)
    act = jax.nn.silu(hidden).astype(jnp.bfloat16)
    output = jnp.einsum("rf,fqc->qrc", act, w_out_q, preferred_element_type=jnp.float32)
    score = jnp.sum(output * all_u.astype(jnp.float32), axis=(0, 2))
    scaled = (rows_p.astype(jnp.float32)[None, :, None] * all_u.astype(jnp.float32)).astype(
        jnp.bfloat16
    )
    back = jnp.einsum("qrc,fqc->rf", scaled, w_out_q, preferred_element_type=jnp.float32)
    sigma = jax.nn.sigmoid(hidden)
    inner = (sigma * (1.0 + hidden * (1.0 - sigma)) * back).astype(jnp.bfloat16)
    grad_out = jnp.einsum("rf,qrc->fqc", act, scaled, preferred_element_type=jnp.float32)
    grad_in = jnp.einsum("qrc,rf->qcf", all_x, inner, preferred_element_type=jnp.float32)
    row_grad = jnp.einsum("rf,qcf->qrc", inner, w_in_q, preferred_element_type=jnp.float32)
    return (
        row_grad,
        score,
        grad_in.reshape(quarters * part, ff),
        grad_out.reshape(ff, quarters * part),
    )


def per_device(tokens, cotangent, probs, expert_ids, w_in, w_out):
    count, top = expert_ids.shape
    width = tokens.shape[1]
    n_dp = lax.axis_size("dp")
    part = width // n_dp
    d = lax.axis_index("dp")
    experts = lax.axis_size("expert") * w_in.shape[0]
    capacity = min(count, max(2, (9 * top * count + 8 * experts - 1) // (8 * experts)))
    block_in = w_in[0]
    block_out = w_out[0]
    target, placing, picker = slot_tables(expert_ids, capacity, experts)
    pick = picker.astype(jnp.bfloat16)
    x_part = lax.dynamic_slice_in_dim(tokens, d * part, part, axis=1)
    u_part = lax.dynamic_slice_in_dim(cotangent, d * part, part, axis=1)
    slot_x = lax.dot_general(
        pick, x_part, (((0,), (0,)), ((), ())), preferred_element_type=jnp.float32
    )
    slot_u = lax.dot_general(
        pick, u_part, (((0,), (0,)), ((), ())), preferred_element_type=jnp.float32
    )
    slot_p = jnp.dot(
        probs.reshape(-1).astype(jnp.float32), placing, precision=lax.Precision.HIGHEST
    )
    slot_x = slot_x.astype(jnp.bfloat16).reshape(experts, capacity, part)
    slot_u = slot_u.astype(jnp.bfloat16).reshape(experts, capacity, part)
    slot_p = slot_p.astype(jnp.bfloat16).reshape(experts, capacity)
    recv_x, recv_u, recv_p = (
        lax.all_to_all(slot_x, "expert", split_axis=0, concat_axis=0, tiled=True),
        lax.all_to_all(slot_u, "expert", split_axis=0, concat_axis=0, tiled=True),
        lax.all_to_all(slot_p, "expert", split_axis=0, concat_axis=0, tiled=True),
    )
    rows = recv_p.size
    all_x = lax.all_gather(recv_x.reshape(rows, part), "dp", axis=0, tiled=False)
    all_u = lax.all_gather(recv_u.reshape(rows, part), "dp", axis=0, tiled=False)
    row_grad, score, grad_in, grad_out = expert_terms(
        all_x, all_u, recv_p.reshape(rows), block_in, block_out
    )
    mixed = lax.all_to_all(
        row_grad.astype(jnp.bfloat16), "dp", split_axis=0, concat_axis=0, tiled=True
    )
    row_sum = jnp.sum(mixed.astype(jnp.float32), axis=0).astype(jnp.bfloat16)
    score_all = lax.all_gather(score.astype(jnp.bfloat16), "dp", axis=0, tiled=False)
    score_sum = jnp.sum(score_all.astype(jnp.float32), axis=0)
    back_x, back_s = (
        lax.all_to_all(
            row_sum.reshape(experts, capacity, part), "expert", split_axis=0, concat_axis=0,
            tiled=True,
        ),
        lax.all_to_all(
            score_sum.astype(jnp.bfloat16).reshape(experts, capacity), "expert", split_axis=0,
            concat_axis=0, tiled=True,
        ),
    )
    token_part = jnp.dot(
        pick, back_x.reshape(experts * capacity, part), preferred_element_type=jnp.float32
    )
    grad_tokens = lax.all_gather(token_part.astype(jnp.bfloat16), "dp", axis=1, tiled=True)
    gate_grad = (
        jnp.take(back_s.reshape(-1).astype(jnp.float32), target).reshape(count, top)
    ).astype(jnp.bfloat16)
    grad_w_in = grad_in.astype(jnp.bfloat16)[None]
    grad_w_out = grad_out.astype(jnp.bfloat16)[None]
    return (grad_tokens, gate_grad, grad_w_in, grad_w_out)


def solution(mesh):
    in_specs = (
        P("expert", None),
        P("expert", None),
        P("expert", None),
        P("expert", None),
        P("expert", None, "dp"),
        P("expert", "dp", None),
    )
    out_specs = (
        P("expert", None),
        P("expert", None),
        P("expert", None, "dp"),
        P("expert", "dp", None),
    )
    return jax.shard_map(
        per_device, mesh=mesh, in_specs=in_specs, out_specs=out_specs, check_vma=False
    )
```

```python
import jax
import jax.numpy as jnp
from jax import lax
from jax.sharding import Mesh
from jax.sharding import PartitionSpec as P

DP = ("zlo", "core")


def slot_tables(expert_ids, capacity, experts):
    count, top = expert_ids.shape
    pairs = count * top
    flat = expert_ids.reshape(pairs)
    onehot = flat[:, None] == jnp.arange(experts, dtype=jnp.int32)[None, :]
    earlier = (
        jnp.arange(pairs, dtype=jnp.int32)[None, :] < jnp.arange(pairs, dtype=jnp.int32)[:, None]
    ).astype(jnp.bfloat16)
    counts = jnp.dot(earlier, onehot.astype(jnp.bfloat16), preferred_element_type=jnp.float32)
    slot = jnp.sum(jnp.where(onehot, counts, 0.0), axis=1).astype(jnp.int32)
    target = flat * capacity + slot
    placing = (target[:, None] == jnp.arange(experts * capacity, dtype=jnp.int32)[None, :]).astype(
        jnp.float32
    )
    picker = jnp.sum(placing.reshape(count, top, experts * capacity), axis=1)
    return (target, placing, picker)


def expert_terms(all_x, all_u, rows_p, block_in, block_out):
    n_c, n_z, rows, part = all_x.shape
    ff = block_in.shape[1]
    w_in_q = block_in.reshape(n_z, n_c, part, ff)
    w_out_q = block_out.reshape(ff, n_z, n_c, part)
    hidden = jnp.einsum("czrk,zckf->rf", all_x, w_in_q, preferred_element_type=jnp.float32)
    act = jax.nn.silu(hidden).astype(jnp.bfloat16)
    output = jnp.einsum("rf,fzck->czrk", act, w_out_q, preferred_element_type=jnp.float32)
    score = jnp.sum(output * all_u.astype(jnp.float32), axis=(0, 1, 3))
    scaled = (
        rows_p.astype(jnp.float32)[None, None, :, None] * all_u.astype(jnp.float32)
    ).astype(jnp.bfloat16)
    back = jnp.einsum("czrk,fzck->rf", scaled, w_out_q, preferred_element_type=jnp.float32)
    sigma = jax.nn.sigmoid(hidden)
    inner = (sigma * (1.0 + hidden * (1.0 - sigma)) * back).astype(jnp.bfloat16)
    grad_out = jnp.einsum("rf,czrk->fzck", act, scaled, preferred_element_type=jnp.float32)
    grad_in = jnp.einsum("czrk,rf->zckf", all_x, inner, preferred_element_type=jnp.float32)
    row_grad = jnp.einsum("rf,zckf->zcrk", inner, w_in_q, preferred_element_type=jnp.float32)
    return (
        row_grad,
        score,
        grad_in.reshape(n_z * n_c * part, ff),
        grad_out.reshape(ff, n_z * n_c * part),
    )


def per_device(tokens, cotangent, probs, expert_ids, w_in, w_out):
    count, top = expert_ids.shape
    width = tokens.shape[1]
    n_z = lax.axis_size("zlo")
    n_c = lax.axis_size("core")
    part = width // (n_z * n_c)
    d = lax.axis_index("zlo") * n_c + lax.axis_index("core")
    experts = lax.axis_size("expert") * w_in.shape[0]
    capacity = min(count, max(2, (9 * top * count + 8 * experts - 1) // (8 * experts)))
    block_in = w_in[0]
    block_out = w_out[0]
    target, placing, picker = slot_tables(expert_ids, capacity, experts)
    pick = picker.astype(jnp.bfloat16)
    x_part = lax.dynamic_slice_in_dim(tokens, d * part, part, axis=1)
    u_part = lax.dynamic_slice_in_dim(cotangent, d * part, part, axis=1)
    xu = jnp.concatenate([x_part, u_part], axis=1)
    slot_xu = lax.dot_general(
        pick, xu, (((0,), (0,)), ((), ())), preferred_element_type=jnp.float32
    ).astype(jnp.bfloat16)
    slot_p = jnp.dot(
        probs.reshape(-1).astype(jnp.float32), placing, precision=lax.Precision.HIGHEST
    ).astype(jnp.bfloat16)
    pad = jnp.zeros((experts * capacity, 127), jnp.bfloat16)
    packed = jnp.concatenate([slot_xu, slot_p[:, None], pad], axis=1)
    packed = packed.reshape(experts, capacity, packed.shape[1])
    recv = lax.all_to_all(packed, "expert", split_axis=0, concat_axis=0, tiled=True)
    rows = experts * capacity
    recv = recv.reshape(rows, recv.shape[2])
    recv_xu = recv[:, : 2 * part]
    recv_p = recv[:, 2 * part]
    pair_xu = lax.all_gather(recv_xu, "zlo", axis=0, tiled=False)
    all_xu = lax.all_gather(pair_xu, "core", axis=0, tiled=False)
    all_x = all_xu[..., :part]
    all_u = all_xu[..., part:]
    row_grad, score, grad_in, grad_out = expert_terms(all_x, all_u, recv_p, block_in, block_out)
    on_chip = lax.all_to_all(
        row_grad.astype(jnp.bfloat16), "core", split_axis=1, concat_axis=1, tiled=True
    )
    chip_sum = jnp.sum(on_chip.astype(jnp.float32), axis=1).astype(jnp.bfloat16)
    off_chip = lax.all_to_all(chip_sum, "zlo", split_axis=0, concat_axis=0, tiled=True)
    row_sum = jnp.sum(off_chip.astype(jnp.float32), axis=0).astype(jnp.bfloat16)
    score_all = lax.all_gather(score.astype(jnp.bfloat16), DP, axis=0, tiled=False)
    score_sum = jnp.sum(score_all.astype(jnp.float32), axis=0)
    back_x, back_s = (
        lax.all_to_all(
            row_sum.reshape(experts, capacity, part), "expert", split_axis=0, concat_axis=0,
            tiled=True,
        ),
        lax.all_to_all(
            score_sum.astype(jnp.bfloat16).reshape(experts, capacity), "expert", split_axis=0,
            concat_axis=0, tiled=True,
        ),
    )
    token_part = jnp.dot(
        pick, back_x.reshape(experts * capacity, part), preferred_element_type=jnp.float32
    )
    grad_tokens = lax.all_gather(token_part.astype(jnp.bfloat16), DP, axis=1, tiled=True)
    gate_grad = (
        jnp.take(back_s.reshape(-1).astype(jnp.float32), target).reshape(count, top)
    ).astype(jnp.bfloat16)
    grad_w_in = grad_in.astype(jnp.bfloat16)[None]
    grad_w_out = grad_out.astype(jnp.bfloat16)[None]
    return (grad_tokens, gate_grad, grad_w_in, grad_w_out)


def solution(mesh):
    n_dp, n_ex = mesh.devices.shape
    split = Mesh(mesh.devices.reshape(2, n_dp // 2, n_ex), ("zlo", "core", "expert"))
    in_specs = (
        P("expert", None),
        P("expert", None),
        P("expert", None),
        P("expert", None),
        P("expert", None, DP),
        P("expert", DP, None),
    )
    out_specs = (
        P("expert", None),
        P("expert", None),
        P("expert", None, DP),
        P("expert", DP, None),
    )
    return jax.shard_map(
        per_device, mesh=split, in_specs=in_specs, out_specs=out_specs, check_vma=False
    )
```

```python
import jax
import jax.numpy as jnp
from jax import lax
from jax.sharding import Mesh
from jax.sharding import PartitionSpec as P

DP = ("zlo", "core")


def slot_tables(expert_ids, capacity, experts):
    count, top = expert_ids.shape
    pairs = count * top
    flat = expert_ids.reshape(pairs)
    onehot = flat[:, None] == jnp.arange(experts, dtype=jnp.int32)[None, :]
    earlier = (
        jnp.arange(pairs, dtype=jnp.int32)[None, :] < jnp.arange(pairs, dtype=jnp.int32)[:, None]
    ).astype(jnp.bfloat16)
    counts = jnp.dot(earlier, onehot.astype(jnp.bfloat16), preferred_element_type=jnp.float32)
    slot = jnp.sum(jnp.where(onehot, counts, 0.0), axis=1).astype(jnp.int32)
    target = flat * capacity + slot
    placing = (target[:, None] == jnp.arange(experts * capacity, dtype=jnp.int32)[None, :]).astype(
        jnp.float32
    )
    picker = jnp.sum(placing.reshape(count, top, experts * capacity), axis=1)
    return (target, placing, picker)


def expert_terms(all_x, all_u, rows_p, block_in, block_out):
    n_c, n_z, rows, part = all_x.shape
    ff = block_in.shape[1]
    w_in_q = block_in.reshape(n_z, n_c, part, ff)
    w_out_q = block_out.reshape(ff, n_z, n_c, part)
    hidden = jnp.einsum("czrk,zckf->rf", all_x, w_in_q, preferred_element_type=jnp.float32)
    act = jax.nn.silu(hidden).astype(jnp.bfloat16)
    output = jnp.einsum("rf,fzck->czrk", act, w_out_q, preferred_element_type=jnp.float32)
    score = jnp.sum(output * all_u.astype(jnp.float32), axis=(0, 1, 3))
    scaled = (
        rows_p.astype(jnp.float32)[None, None, :, None] * all_u.astype(jnp.float32)
    ).astype(jnp.bfloat16)
    back = jnp.einsum("czrk,fzck->rf", scaled, w_out_q, preferred_element_type=jnp.float32)
    sigma = jax.nn.sigmoid(hidden)
    inner = (sigma * (1.0 + hidden * (1.0 - sigma)) * back).astype(jnp.bfloat16)
    grad_out = jnp.einsum("rf,czrk->fzck", act, scaled, preferred_element_type=jnp.float32)
    grad_in = jnp.einsum("czrk,rf->zckf", all_x, inner, preferred_element_type=jnp.float32)
    row_grad = jnp.einsum("rf,zckf->zcrk", inner, w_in_q, preferred_element_type=jnp.float32)
    return (
        row_grad,
        score,
        grad_in.reshape(n_z * n_c * part, ff),
        grad_out.reshape(ff, n_z * n_c * part),
    )


def per_device(tokens, cotangent, probs, expert_ids, w_in, w_out):
    count, top = expert_ids.shape
    width = tokens.shape[1]
    n_z = lax.axis_size("zlo")
    n_c = lax.axis_size("core")
    part = width // (n_z * n_c)
    d = lax.axis_index("zlo") * n_c + lax.axis_index("core")
    experts = lax.axis_size("expert") * w_in.shape[0]
    capacity = min(count, max(2, (9 * top * count + 8 * experts - 1) // (8 * experts)))
    block_in = w_in[0]
    block_out = w_out[0]
    target, placing, picker = slot_tables(expert_ids, capacity, experts)
    pick = picker.astype(jnp.bfloat16)
    x_part = lax.dynamic_slice_in_dim(tokens, d * part, part, axis=1)
    u_part = lax.dynamic_slice_in_dim(cotangent, d * part, part, axis=1)
    xu = jnp.concatenate([x_part, u_part], axis=1)
    slot_xu = lax.dot_general(
        pick, xu, (((0,), (0,)), ((), ())), preferred_element_type=jnp.float32
    ).astype(jnp.bfloat16)
    slot_p = jnp.dot(
        probs.reshape(-1).astype(jnp.float32), placing, precision=lax.Precision.HIGHEST
    ).astype(jnp.bfloat16)
    pad = jnp.zeros((experts * capacity, 127), jnp.bfloat16)
    packed = jnp.concatenate([slot_xu, slot_p[:, None], pad], axis=1)
    lanes = packed.shape[1]
    packed = packed.reshape(experts, capacity * lanes // 128, 128)
    recv = lax.all_to_all(packed, "expert", split_axis=0, concat_axis=0, tiled=True)
    rows = experts * capacity
    recv = recv.reshape(rows, lanes)
    recv_xu = recv[:, : 2 * part]
    recv_p = recv[:, 2 * part]
    pair_xu = lax.all_gather(recv_xu, "zlo", axis=0, tiled=False)
    all_xu = lax.all_gather(pair_xu, "core", axis=0, tiled=False)
    all_x = all_xu[..., :part]
    all_u = all_xu[..., part:]
    row_grad, score, grad_in, grad_out = expert_terms(all_x, all_u, recv_p, block_in, block_out)
    on_chip = lax.all_to_all(
        row_grad.astype(jnp.bfloat16), "core", split_axis=1, concat_axis=1, tiled=True
    )
    chip_sum = jnp.sum(on_chip.astype(jnp.float32), axis=1).astype(jnp.bfloat16)
    off_chip = lax.all_to_all(chip_sum, "zlo", split_axis=0, concat_axis=0, tiled=True)
    row_sum = jnp.sum(off_chip.astype(jnp.float32), axis=0).astype(jnp.bfloat16)
    score_all = lax.all_gather(score.astype(jnp.bfloat16), DP, axis=0, tiled=False)
    score_sum = jnp.sum(score_all.astype(jnp.float32), axis=0)
    back_x, back_s = (
        lax.all_to_all(
            row_sum.reshape(experts, capacity * part // 128, 128), "expert", split_axis=0,
            concat_axis=0, tiled=True,
        ),
        lax.all_to_all(
            score_sum.astype(jnp.bfloat16).reshape(experts, capacity), "expert", split_axis=0,
            concat_axis=0, tiled=True,
        ),
    )
    token_part = jnp.dot(
        pick, back_x.reshape(experts * capacity, part), preferred_element_type=jnp.float32
    )
    grad_tokens = lax.all_gather(token_part.astype(jnp.bfloat16), DP, axis=1, tiled=True)
    gate_grad = (
        jnp.take(back_s.reshape(-1).astype(jnp.float32), target).reshape(count, top)
    ).astype(jnp.bfloat16)
    grad_w_in = grad_in.astype(jnp.bfloat16)[None]
    grad_w_out = grad_out.astype(jnp.bfloat16)[None]
    return (grad_tokens, gate_grad, grad_w_in, grad_w_out)


def solution(mesh):
    n_dp, n_ex = mesh.devices.shape
    split = Mesh(mesh.devices.reshape(2, n_dp // 2, n_ex), ("zlo", "core", "expert"))
    in_specs = (
        P("expert", None),
        P("expert", None),
        P("expert", None),
        P("expert", None),
        P("expert", None, DP),
        P("expert", DP, None),
    )
    out_specs = (
        P("expert", None),
        P("expert", None),
        P("expert", None, DP),
        P("expert", DP, None),
    )
    return jax.shard_map(
        per_device, mesh=split, in_specs=in_specs, out_specs=out_specs, check_vma=False
    )
```

```python
import jax
import jax.numpy as jnp
from jax import lax
from jax.sharding import Mesh
from jax.sharding import PartitionSpec as P

DP = ("zlo", "core")


def slot_tables(expert_ids, capacity, experts):
    count, top = expert_ids.shape
    pairs = count * top
    flat = expert_ids.reshape(pairs)
    onehot = flat[:, None] == jnp.arange(experts, dtype=jnp.int32)[None, :]
    earlier = (
        jnp.arange(pairs, dtype=jnp.int32)[None, :] < jnp.arange(pairs, dtype=jnp.int32)[:, None]
    ).astype(jnp.bfloat16)
    counts = jnp.dot(earlier, onehot.astype(jnp.bfloat16), preferred_element_type=jnp.float32)
    slot = jnp.sum(jnp.where(onehot, counts, 0.0), axis=1).astype(jnp.int32)
    target = flat * capacity + slot
    placing = (target[:, None] == jnp.arange(experts * capacity, dtype=jnp.int32)[None, :]).astype(
        jnp.float32
    )
    picker = jnp.sum(placing.reshape(count, top, experts * capacity), axis=1)
    return (target, placing, picker)


def expert_terms(all_x, all_u, rows_p, block_in, block_out, quarters):
    halves, rows, half = all_x.shape
    ff = block_in.shape[1]
    w_in_h = block_in.reshape(halves, half, ff)
    w_out_h = block_out.reshape(ff, halves, half)
    hidden = jnp.einsum("hrk,hkf->rf", all_x, w_in_h, preferred_element_type=jnp.float32)
    act = jax.nn.silu(hidden).astype(jnp.bfloat16)
    output = jnp.einsum("rf,fhk->hrk", act, w_out_h, preferred_element_type=jnp.float32)
    score = jnp.sum(output * all_u.astype(jnp.float32), axis=(0, 2))
    scaled = (rows_p.astype(jnp.float32)[None, :, None] * all_u.astype(jnp.float32)).astype(
        jnp.bfloat16
    )
    back = jnp.einsum("hrk,fhk->rf", scaled, w_out_h, preferred_element_type=jnp.float32)
    sigma = jax.nn.sigmoid(hidden)
    inner = (sigma * (1.0 + hidden * (1.0 - sigma)) * back).astype(jnp.bfloat16)
    grad_out = jnp.einsum("rf,hrk->fhk", act, scaled, preferred_element_type=jnp.float32)
    grad_in = jnp.einsum("hrk,rf->hkf", all_x, inner, preferred_element_type=jnp.float32)
    w_in_q = block_in.reshape(quarters, halves * half // quarters, ff)
    row_grad = jnp.einsum("rf,qkf->qrk", inner, w_in_q, preferred_element_type=jnp.float32)
    return (
        row_grad,
        score,
        grad_in.reshape(halves * half, ff),
        grad_out.reshape(ff, halves * half),
    )


def per_device(tokens, cotangent, probs, expert_ids, w_in, w_out):
    count, top = expert_ids.shape
    width = tokens.shape[1]
    n_z = lax.axis_size("zlo")
    n_c = lax.axis_size("core")
    part = width // (n_z * n_c)
    d = lax.axis_index("zlo") * n_c + lax.axis_index("core")
    experts = lax.axis_size("expert") * w_in.shape[0]
    capacity = min(count, max(2, (9 * top * count + 8 * experts - 1) // (8 * experts)))
    block_in = w_in[0]
    block_out = w_out[0]
    target, placing, picker = slot_tables(expert_ids, capacity, experts)
    pick = picker.astype(jnp.bfloat16)
    c = lax.axis_index("core")
    half = width // n_c
    x_half = lax.dynamic_slice_in_dim(tokens, c * half, half, axis=1)
    u_half = lax.dynamic_slice_in_dim(cotangent, c * half, half, axis=1)
    xu = jnp.concatenate([x_half, u_half], axis=1)
    slot_xu = lax.dot_general(
        pick, xu, (((0,), (0,)), ((), ())), preferred_element_type=jnp.float32
    ).astype(jnp.bfloat16)
    slot_p = jnp.dot(
        probs.reshape(-1).astype(jnp.float32), placing, precision=lax.Precision.HIGHEST
    ).astype(jnp.bfloat16)
    body = capacity * 2 * half // 128
    packed = jnp.concatenate(
        [
            slot_xu.reshape(experts, body, 128),
            jnp.pad(slot_p.reshape(experts, 1, capacity), ((0, 0), (0, 0), (0, 128 - capacity))),
        ],
        axis=1,
    )
    recv = lax.all_to_all(packed, "expert", split_axis=0, concat_axis=0, tiled=True)
    rows = experts * capacity
    recv_xu = recv[:, :body, :].reshape(rows, 2 * half)
    recv_p = recv[:, body, :capacity].reshape(rows)
    all_xu = lax.all_gather(recv_xu, "core", axis=0, tiled=False)
    all_x = all_xu[..., :half]
    all_u = all_xu[..., half:]
    row_grad, score, grad_in, grad_out = expert_terms(
        all_x, all_u, recv_p, block_in, block_out, n_z * n_c
    )
    on_chip = lax.all_to_all(
        row_grad.astype(jnp.bfloat16).reshape(n_z, n_c, rows, part), "core", split_axis=1, concat_axis=1, tiled=True
    )
    chip_sum = jnp.sum(on_chip.astype(jnp.float32), axis=1).astype(jnp.bfloat16)
    off_chip = lax.all_to_all(chip_sum, "zlo", split_axis=0, concat_axis=0, tiled=True)
    row_sum = jnp.sum(off_chip.astype(jnp.float32), axis=0).astype(jnp.bfloat16)
    score_all = lax.all_gather(score.astype(jnp.bfloat16), DP, axis=0, tiled=False)
    score_sum = jnp.sum(score_all.astype(jnp.float32), axis=0)
    back_x, back_s = (
        lax.all_to_all(
            row_sum.reshape(experts, capacity * part // 128, 128), "expert", split_axis=0,
            concat_axis=0, tiled=True,
        ),
        lax.all_to_all(
            score_sum.astype(jnp.bfloat16).reshape(experts, capacity), "expert", split_axis=0,
            concat_axis=0, tiled=True,
        ),
    )
    token_part = jnp.dot(
        pick, back_x.reshape(experts * capacity, part), preferred_element_type=jnp.float32
    )
    grad_tokens = lax.all_gather(token_part.astype(jnp.bfloat16), DP, axis=1, tiled=True)
    gate_grad = (
        jnp.take(back_s.reshape(-1).astype(jnp.float32), target).reshape(count, top)
    ).astype(jnp.bfloat16)
    grad_w_in = grad_in.astype(jnp.bfloat16)[None]
    grad_w_out = grad_out.astype(jnp.bfloat16)[None]
    return (grad_tokens, gate_grad, grad_w_in, grad_w_out)


def solution(mesh):
    n_dp, n_ex = mesh.devices.shape
    split = Mesh(mesh.devices.reshape(2, n_dp // 2, n_ex), ("zlo", "core", "expert"))
    in_specs = (
        P("expert", None),
        P("expert", None),
        P("expert", None),
        P("expert", None),
        P("expert", None, DP),
        P("expert", DP, None),
    )
    out_specs = (
        P("expert", None),
        P("expert", None),
        P("expert", None, DP),
        P("expert", DP, None),
    )
    return jax.shard_map(
        per_device, mesh=split, in_specs=in_specs, out_specs=out_specs, check_vma=False
    )
```

```python
import jax
import jax.numpy as jnp
from jax import lax
from jax.sharding import Mesh
from jax.sharding import PartitionSpec as P

DP = ("zlo", "core")


def slot_tables(expert_ids, capacity, experts):
    count, top = expert_ids.shape
    pairs = count * top
    flat = expert_ids.reshape(pairs)
    onehot = flat[:, None] == jnp.arange(experts, dtype=jnp.int32)[None, :]
    earlier = (
        jnp.arange(pairs, dtype=jnp.int32)[None, :] < jnp.arange(pairs, dtype=jnp.int32)[:, None]
    ).astype(jnp.bfloat16)
    counts = jnp.dot(earlier, onehot.astype(jnp.bfloat16), preferred_element_type=jnp.float32)
    slot = jnp.sum(jnp.where(onehot, counts, 0.0), axis=1).astype(jnp.int32)
    target = flat * capacity + slot
    placing = (target[:, None] == jnp.arange(experts * capacity, dtype=jnp.int32)[None, :]).astype(
        jnp.float32
    )
    picker = jnp.sum(placing.reshape(count, top, experts * capacity), axis=1)
    return (target, placing, picker)


def expert_terms(all_x, all_u, rows_p, block_in, block_out, quarters):
    halves, rows, half = all_x.shape
    ff = block_in.shape[1]
    w_in_h = block_in.reshape(halves, half, ff)
    w_out_h = block_out.reshape(ff, halves, half)
    hidden = jnp.einsum("hrk,hkf->rf", all_x, w_in_h, preferred_element_type=jnp.float32)
    act = jax.nn.silu(hidden).astype(jnp.bfloat16)
    output = jnp.einsum("rf,fhk->hrk", act, w_out_h, preferred_element_type=jnp.float32)
    score = jnp.sum(output * all_u.astype(jnp.float32), axis=(0, 2))
    scaled = (rows_p.astype(jnp.float32)[None, :, None] * all_u.astype(jnp.float32)).astype(
        jnp.bfloat16
    )
    back = jnp.einsum("hrk,fhk->rf", scaled, w_out_h, preferred_element_type=jnp.float32)
    sigma = jax.nn.sigmoid(hidden)
    inner = (sigma * (1.0 + hidden * (1.0 - sigma)) * back).astype(jnp.bfloat16)
    grad_out = jnp.einsum("rf,hrk->fhk", act, scaled, preferred_element_type=jnp.float32)
    grad_in = jnp.einsum("hrk,rf->hkf", all_x, inner, preferred_element_type=jnp.float32)
    w_in_q = block_in.reshape(quarters, halves * half // quarters, ff)
    row_grad = jnp.einsum("rf,qkf->qrk", inner, w_in_q, preferred_element_type=jnp.float32)
    return (
        row_grad,
        score,
        grad_in.reshape(halves * half, ff),
        grad_out.reshape(ff, halves * half),
    )


def per_device(tokens, cotangent, probs, expert_ids, w_in, w_out):
    count, top = expert_ids.shape
    width = tokens.shape[1]
    n_z = lax.axis_size("zlo")
    n_c = lax.axis_size("core")
    part = width // (n_z * n_c)
    d = lax.axis_index("zlo") * n_c + lax.axis_index("core")
    experts = lax.axis_size("expert") * w_in.shape[0]
    capacity = min(count, max(2, (9 * top * count + 8 * experts - 1) // (8 * experts)))
    block_in = w_in[0]
    block_out = w_out[0]
    target, placing, picker = slot_tables(expert_ids, capacity, experts)
    pick = picker.astype(jnp.bfloat16)
    c = lax.axis_index("core")
    half = width // n_c
    x_half = lax.dynamic_slice_in_dim(tokens, c * half, half, axis=1)
    u_half = lax.dynamic_slice_in_dim(cotangent, c * half, half, axis=1)
    xu = jnp.concatenate([x_half, u_half], axis=1)
    slot_xu = lax.dot_general(
        pick, xu, (((0,), (0,)), ((), ())), preferred_element_type=jnp.float32
    ).astype(jnp.bfloat16)
    slot_p = jnp.dot(
        probs.reshape(-1).astype(jnp.float32), placing, precision=lax.Precision.HIGHEST
    ).astype(jnp.bfloat16)
    body = capacity * 2 * half // 128
    packed = jnp.concatenate(
        [
            slot_xu.reshape(experts, body, 128),
            jnp.pad(slot_p.reshape(experts, 1, capacity), ((0, 0), (0, 0), (0, 128 - capacity))),
        ],
        axis=1,
    )
    recv = lax.all_to_all(packed, "expert", split_axis=0, concat_axis=0, tiled=True)
    rows = experts * capacity
    recv_xu = recv[:, :body, :].reshape(rows, 2 * half)
    recv_p = recv[:, body, :capacity].reshape(rows)
    all_xu = lax.all_gather(recv_xu, "core", axis=0, tiled=False)
    all_x = all_xu[..., :half]
    all_u = all_xu[..., half:]
    row_grad, score, grad_in, grad_out = expert_terms(
        all_x, all_u, recv_p, block_in, block_out, n_z * n_c
    )
    rg = row_grad.astype(jnp.bfloat16).reshape(n_z, n_c, rows, part)
    nrow = -(-rows // part)
    srow = jnp.pad(score.astype(jnp.bfloat16), (0, nrow * part - rows)).reshape(1, 1, nrow, part)
    chunk = jnp.concatenate([rg, jnp.broadcast_to(srow, (n_z, n_c, nrow, part))], axis=2)
    on_chip = lax.all_to_all(chunk, "core", split_axis=1, concat_axis=1, tiled=True)
    chip_sum = jnp.sum(on_chip[:, :, :rows].astype(jnp.float32), axis=1).astype(jnp.bfloat16)
    chip_scores = on_chip[:, :, rows:].reshape(n_z, n_c * nrow, part)
    chunk2 = jnp.concatenate([chip_sum, chip_scores], axis=1)
    off_chip = lax.all_to_all(chunk2, "zlo", split_axis=0, concat_axis=0, tiled=True)
    row_sum = jnp.sum(off_chip[:, :rows].astype(jnp.float32), axis=0).astype(jnp.bfloat16)
    block_scores = off_chip[:, rows:].reshape(n_z * n_c, nrow * part)[:, :rows]
    score_sum = jnp.sum(block_scores.astype(jnp.float32), axis=0)
    body2 = capacity * part // 128
    packed2 = jnp.concatenate(
        [
            row_sum.reshape(experts, body2, 128),
            jnp.pad(
                score_sum.astype(jnp.bfloat16).reshape(experts, 1, capacity),
                ((0, 0), (0, 0), (0, 128 - capacity)),
            ),
        ],
        axis=1,
    )
    back = lax.all_to_all(packed2, "expert", split_axis=0, concat_axis=0, tiled=True)
    back_x = back[:, :body2, :]
    back_s = back[:, body2, :capacity]
    token_part = jnp.dot(
        pick, back_x.reshape(experts * capacity, part), preferred_element_type=jnp.float32
    )
    grad_tokens = lax.all_gather(token_part.astype(jnp.bfloat16), DP, axis=1, tiled=True)
    gate_grad = (
        jnp.take(back_s.reshape(-1).astype(jnp.float32), target).reshape(count, top)
    ).astype(jnp.bfloat16)
    grad_w_in = grad_in.astype(jnp.bfloat16)[None]
    grad_w_out = grad_out.astype(jnp.bfloat16)[None]
    return (grad_tokens, gate_grad, grad_w_in, grad_w_out)


def solution(mesh):
    n_dp, n_ex = mesh.devices.shape
    split = Mesh(mesh.devices.reshape(2, n_dp // 2, n_ex), ("zlo", "core", "expert"))
    in_specs = (
        P("expert", None),
        P("expert", None),
        P("expert", None),
        P("expert", None),
        P("expert", None, DP),
        P("expert", DP, None),
    )
    out_specs = (
        P("expert", None),
        P("expert", None),
        P("expert", None, DP),
        P("expert", DP, None),
    )
    return jax.shard_map(
        per_device, mesh=split, in_specs=in_specs, out_specs=out_specs, check_vma=False
    )
```

```python
import jax
import jax.numpy as jnp
from jax import lax
from jax.sharding import Mesh
from jax.sharding import PartitionSpec as P

DP = ("zlo", "core")


def slot_tables(expert_ids, capacity, experts):
    count, top = expert_ids.shape
    pairs = count * top
    flat = expert_ids.reshape(pairs)
    onehot = flat[:, None] == jnp.arange(experts, dtype=jnp.int32)[None, :]
    earlier = (
        jnp.arange(pairs, dtype=jnp.int32)[None, :] < jnp.arange(pairs, dtype=jnp.int32)[:, None]
    ).astype(jnp.bfloat16)
    counts = jnp.dot(earlier, onehot.astype(jnp.bfloat16), preferred_element_type=jnp.float32)
    slot = jnp.sum(jnp.where(onehot, counts, 0.0), axis=1).astype(jnp.int32)
    target = flat * capacity + slot
    placing = (target[:, None] == jnp.arange(experts * capacity, dtype=jnp.int32)[None, :]).astype(
        jnp.float32
    )
    picker = jnp.sum(placing.reshape(count, top, experts * capacity), axis=1)
    return (target, placing, picker)


def expert_terms(all_x, all_u, rows_p, block_in, block_out, quarters):
    halves, rows, half = all_x.shape
    ff = block_in.shape[1]
    w_in_h = block_in.reshape(halves, half, ff)
    w_out_h = block_out.reshape(ff, halves, half)
    hidden = jnp.einsum("hrk,hkf->rf", all_x, w_in_h, preferred_element_type=jnp.float32)
    act = jax.nn.silu(hidden).astype(jnp.bfloat16)
    output = jnp.einsum("rf,fhk->hrk", act, w_out_h, preferred_element_type=jnp.float32)
    score = jnp.sum(output * all_u.astype(jnp.float32), axis=(0, 2))
    scaled = (rows_p.astype(jnp.float32)[None, :, None] * all_u.astype(jnp.float32)).astype(
        jnp.bfloat16
    )
    back = jnp.einsum("hrk,fhk->rf", scaled, w_out_h, preferred_element_type=jnp.float32)
    sigma = jax.nn.sigmoid(hidden)
    inner = (sigma * (1.0 + hidden * (1.0 - sigma)) * back).astype(jnp.bfloat16)
    grad_out = jnp.einsum("rf,hrk->fhk", act, scaled, preferred_element_type=jnp.float32)
    grad_in = jnp.einsum("hrk,rf->hkf", all_x, inner, preferred_element_type=jnp.float32)
    w_in_q = block_in.reshape(quarters, halves * half // quarters, ff)
    row_grad = jnp.einsum("rf,qkf->qrk", inner, w_in_q, preferred_element_type=jnp.float32)
    return (
        row_grad,
        score,
        grad_in.reshape(halves * half, ff),
        grad_out.reshape(ff, halves * half),
    )


def per_device(tokens, cotangent, probs, expert_ids, w_in, w_out):
    count, top = expert_ids.shape
    width = tokens.shape[1]
    n_z = lax.axis_size("zlo")
    n_c = lax.axis_size("core")
    part = width // (n_z * n_c)
    d = lax.axis_index("zlo") * n_c + lax.axis_index("core")
    experts = lax.axis_size("expert") * w_in.shape[0]
    capacity = min(count, max(2, (9 * top * count + 8 * experts - 1) // (8 * experts)))
    block_in = w_in[0]
    block_out = w_out[0]
    target, placing, picker = slot_tables(expert_ids, capacity, experts)
    pick = picker.astype(jnp.bfloat16)
    c = lax.axis_index("core")
    half = width // n_c
    x_half = lax.dynamic_slice_in_dim(tokens, c * half, half, axis=1)
    u_half = lax.dynamic_slice_in_dim(cotangent, c * half, half, axis=1)
    xu = jnp.concatenate([x_half, u_half], axis=1)
    slot_xu = lax.dot_general(
        pick, xu, (((0,), (0,)), ((), ())), preferred_element_type=jnp.float32
    ).astype(jnp.bfloat16)
    slot_p = jnp.dot(
        probs.reshape(-1).astype(jnp.float32), placing, precision=lax.Precision.HIGHEST
    ).astype(jnp.bfloat16)
    body = capacity * 2 * half // 128
    packed = jnp.concatenate(
        [
            slot_xu.reshape(experts, body, 128),
            jnp.pad(slot_p.reshape(experts, 1, capacity), ((0, 0), (0, 0), (0, 128 - capacity))),
        ],
        axis=1,
    )
    recv = lax.all_to_all(packed, "expert", split_axis=0, concat_axis=0, tiled=True)
    rows = experts * capacity
    recv_xu = recv[:, :body, :].reshape(rows, 2 * half)
    recv_p = recv[:, body, :capacity].reshape(rows)
    all_xu = lax.all_gather(recv_xu, "core", axis=0, tiled=False)
    all_x = all_xu[..., :half]
    all_u = all_xu[..., half:]
    row_grad, score, grad_in, grad_out = expert_terms(
        all_x, all_u, recv_p, block_in, block_out, n_z * n_c
    )
    rg = row_grad.astype(jnp.bfloat16).reshape(n_z, n_c, rows, part)
    nrow = -(-rows // (16 * part)) * 16
    srow = jnp.pad(score.astype(jnp.bfloat16), (0, nrow * part - rows)).reshape(1, 1, nrow, part)
    chunk = jnp.concatenate([rg, jnp.broadcast_to(srow, (n_z, n_c, nrow, part))], axis=2)
    on_chip = lax.all_to_all(chunk, "core", split_axis=1, concat_axis=1, tiled=True)
    chip_sum = jnp.sum(on_chip[:, :, :rows].astype(jnp.float32), axis=1).astype(jnp.bfloat16)
    chip_scores = on_chip[:, :, rows:].reshape(n_z, n_c * nrow, part)
    chunk2 = jnp.concatenate([chip_sum, chip_scores], axis=1)
    off_chip = lax.all_to_all(chunk2, "zlo", split_axis=0, concat_axis=0, tiled=True)
    row_sum = jnp.sum(off_chip[:, :rows].astype(jnp.float32), axis=0).astype(jnp.bfloat16)
    block_scores = off_chip[:, rows:].reshape(n_z * n_c, nrow * part)[:, :rows]
    score_sum = jnp.sum(block_scores.astype(jnp.float32), axis=0)
    body2 = capacity * part // 128
    packed2 = jnp.concatenate(
        [
            row_sum.reshape(experts, body2, 128),
            jnp.pad(
                score_sum.astype(jnp.bfloat16).reshape(experts, 1, capacity),
                ((0, 0), (0, 0), (0, 128 - capacity)),
            ),
        ],
        axis=1,
    )
    back = lax.all_to_all(packed2, "expert", split_axis=0, concat_axis=0, tiled=True)
    back_x = back[:, :body2, :]
    back_s = back[:, body2, :capacity]
    token_part = jnp.dot(
        pick, back_x.reshape(experts * capacity, part), preferred_element_type=jnp.float32
    )
    grad_tokens = lax.all_gather(token_part.astype(jnp.bfloat16), DP, axis=1, tiled=True)
    gate_grad = (
        jnp.take(back_s.reshape(-1).astype(jnp.float32), target).reshape(count, top)
    ).astype(jnp.bfloat16)
    grad_w_in = grad_in.astype(jnp.bfloat16)[None]
    grad_w_out = grad_out.astype(jnp.bfloat16)[None]
    return (grad_tokens, gate_grad, grad_w_in, grad_w_out)


def solution(mesh):
    n_dp, n_ex = mesh.devices.shape
    split = Mesh(mesh.devices.reshape(2, n_dp // 2, n_ex), ("zlo", "core", "expert"))
    in_specs = (
        P("expert", None),
        P("expert", None),
        P("expert", None),
        P("expert", None),
        P("expert", None, DP),
        P("expert", DP, None),
    )
    out_specs = (
        P("expert", None),
        P("expert", None),
        P("expert", None, DP),
        P("expert", DP, None),
    )
    return jax.shard_map(
        per_device, mesh=split, in_specs=in_specs, out_specs=out_specs, check_vma=False
    )
```

```python
import jax
import jax.numpy as jnp
from jax import lax
from jax.sharding import Mesh
from jax.sharding import PartitionSpec as P

DP = ("zlo", "core")


def slot_tables(expert_ids, capacity, experts):
    count, top = expert_ids.shape
    pairs = count * top
    flat = expert_ids.reshape(pairs)
    onehot = flat[:, None] == jnp.arange(experts, dtype=jnp.int32)[None, :]
    earlier = (
        jnp.arange(pairs, dtype=jnp.int32)[None, :] < jnp.arange(pairs, dtype=jnp.int32)[:, None]
    ).astype(jnp.bfloat16)
    counts = jnp.dot(earlier, onehot.astype(jnp.bfloat16), preferred_element_type=jnp.float32)
    slot = jnp.sum(jnp.where(onehot, counts, 0.0), axis=1).astype(jnp.int32)
    target = flat * capacity + slot
    placing = (target[:, None] == jnp.arange(experts * capacity, dtype=jnp.int32)[None, :]).astype(
        jnp.float32
    )
    picker = jnp.sum(placing.reshape(count, top, experts * capacity), axis=1)
    return (target, placing, picker)


def expert_terms(all_x, all_u, rows_p, block_in, block_out, quarters):
    halves, rows, half = all_x.shape
    ff = block_in.shape[1]
    w_in_h = block_in.reshape(halves, half, ff)
    w_out_h = block_out.reshape(ff, halves, half)
    hidden = jnp.einsum("hrk,hkf->rf", all_x, w_in_h, preferred_element_type=jnp.float32)
    act = jax.nn.silu(hidden).astype(jnp.bfloat16)
    output = jnp.einsum("rf,fhk->hrk", act, w_out_h, preferred_element_type=jnp.float32)
    score = jnp.sum(output * all_u.astype(jnp.float32), axis=(0, 2))
    scaled = (rows_p.astype(jnp.float32)[None, :, None] * all_u.astype(jnp.float32)).astype(
        jnp.bfloat16
    )
    back = jnp.einsum("hrk,fhk->rf", scaled, w_out_h, preferred_element_type=jnp.float32)
    sigma = jax.nn.sigmoid(hidden)
    inner = (sigma * (1.0 + hidden * (1.0 - sigma)) * back).astype(jnp.bfloat16)
    grad_out = jnp.einsum("rf,hrk->fhk", act, scaled, preferred_element_type=jnp.float32)
    grad_in = jnp.einsum("hrk,rf->hkf", all_x, inner, preferred_element_type=jnp.float32)
    w_in_q = block_in.reshape(quarters, halves * half // quarters, ff)
    row_grad = jnp.einsum("rf,qkf->qrk", inner, w_in_q, preferred_element_type=jnp.float32)
    return (
        row_grad,
        score,
        grad_in.reshape(halves * half, ff),
        grad_out.reshape(ff, halves * half),
    )


def per_device(tokens, cotangent, probs, expert_ids, w_in, w_out):
    count, top = expert_ids.shape
    width = tokens.shape[1]
    n_z = lax.axis_size("zlo")
    n_c = lax.axis_size("core")
    part = width // (n_z * n_c)
    d = lax.axis_index("zlo") * n_c + lax.axis_index("core")
    experts = lax.axis_size("expert") * w_in.shape[0]
    capacity = min(count, max(2, (9 * top * count + 8 * experts - 1) // (8 * experts)))
    block_in = w_in[0]
    block_out = w_out[0]
    target, placing, picker = slot_tables(expert_ids, capacity, experts)
    pick = picker.astype(jnp.bfloat16)
    c = lax.axis_index("core")
    half = width // n_c
    x_half = lax.dynamic_slice_in_dim(tokens, c * half, half, axis=1)
    u_half = lax.dynamic_slice_in_dim(cotangent, c * half, half, axis=1)
    xu = jnp.concatenate([x_half, u_half], axis=1)
    slot_xu = lax.dot_general(
        pick, xu, (((0,), (0,)), ((), ())), preferred_element_type=jnp.float32
    ).astype(jnp.bfloat16)
    slot_p = jnp.dot(
        probs.reshape(-1).astype(jnp.float32), placing, precision=lax.Precision.HIGHEST
    ).astype(jnp.bfloat16)
    body = capacity * 2 * half // 128
    packed = jnp.concatenate(
        [
            slot_xu.reshape(experts, body, 128),
            jnp.pad(slot_p.reshape(experts, 1, capacity), ((0, 0), (0, 0), (0, 128 - capacity))),
        ],
        axis=1,
    )
    recv = lax.all_to_all(packed, "expert", split_axis=0, concat_axis=0, tiled=True)
    rows = experts * capacity
    recv_p = recv[:, body, :capacity].reshape(rows)
    all_xu = lax.all_gather(recv[:, :body, :], "core", axis=0, tiled=False)
    all_xu = all_xu.reshape(n_c, rows, 2 * half)
    all_x = all_xu[..., :half]
    all_u = all_xu[..., half:]
    row_grad, score, grad_in, grad_out = expert_terms(
        all_x, all_u, recv_p, block_in, block_out, n_z * n_c
    )
    rg = row_grad.astype(jnp.bfloat16).reshape(n_z, n_c, rows, part)
    nrow = -(-rows // (16 * part)) * 16
    srow = jnp.pad(score.astype(jnp.bfloat16), (0, nrow * part - rows)).reshape(1, 1, nrow, part)
    chunk = jnp.concatenate([rg, jnp.broadcast_to(srow, (n_z, n_c, nrow, part))], axis=2)
    on_chip = lax.all_to_all(chunk, "core", split_axis=1, concat_axis=1, tiled=True)
    chip_sum = jnp.sum(on_chip[:, :, :rows].astype(jnp.float32), axis=1).astype(jnp.bfloat16)
    chip_scores = on_chip[:, :, rows:].reshape(n_z, n_c * nrow, part)
    chunk2 = jnp.concatenate([chip_sum, chip_scores], axis=1)
    off_chip = lax.all_to_all(chunk2, "zlo", split_axis=0, concat_axis=0, tiled=True)
    row_sum = jnp.sum(off_chip[:, :rows].astype(jnp.float32), axis=0).astype(jnp.bfloat16)
    block_scores = off_chip[:, rows:].reshape(n_z * n_c, nrow * part)[:, :rows]
    score_sum = jnp.sum(block_scores.astype(jnp.float32), axis=0)
    body2 = capacity * part // 128
    packed2 = jnp.concatenate(
        [
            row_sum.reshape(experts, body2, 128),
            jnp.pad(
                score_sum.astype(jnp.bfloat16).reshape(experts, 1, capacity),
                ((0, 0), (0, 0), (0, 128 - capacity)),
            ),
        ],
        axis=1,
    )
    back = lax.all_to_all(packed2, "expert", split_axis=0, concat_axis=0, tiled=True)
    back_x = back[:, :body2, :]
    back_s = back[:, body2, :capacity]
    token_part = jnp.dot(
        pick, back_x.reshape(experts * capacity, part), preferred_element_type=jnp.float32
    )
    grad_tokens = lax.all_gather(token_part.astype(jnp.bfloat16), DP, axis=1, tiled=True)
    gate_grad = (
        jnp.take(back_s.reshape(-1).astype(jnp.float32), target).reshape(count, top)
    ).astype(jnp.bfloat16)
    grad_w_in = grad_in.astype(jnp.bfloat16)[None]
    grad_w_out = grad_out.astype(jnp.bfloat16)[None]
    return (grad_tokens, gate_grad, grad_w_in, grad_w_out)


def solution(mesh):
    n_dp, n_ex = mesh.devices.shape
    split = Mesh(mesh.devices.reshape(2, n_dp // 2, n_ex), ("zlo", "core", "expert"))
    in_specs = (
        P("expert", None),
        P("expert", None),
        P("expert", None),
        P("expert", None),
        P("expert", None, DP),
        P("expert", DP, None),
    )
    out_specs = (
        P("expert", None),
        P("expert", None),
        P("expert", None, DP),
        P("expert", DP, None),
    )
    return jax.shard_map(
        per_device, mesh=split, in_specs=in_specs, out_specs=out_specs, check_vma=False
    )
```

```python
import jax
import jax.numpy as jnp
from jax import lax
from jax.sharding import Mesh
from jax.sharding import PartitionSpec as P

DP = ("zlo", "core")


def slot_tables(expert_ids, capacity, experts):
    count, top = expert_ids.shape
    pairs = count * top
    flat = expert_ids.reshape(pairs)
    onehot = flat[:, None] == jnp.arange(experts, dtype=jnp.int32)[None, :]
    earlier = (
        jnp.arange(pairs, dtype=jnp.int32)[None, :] < jnp.arange(pairs, dtype=jnp.int32)[:, None]
    ).astype(jnp.bfloat16)
    counts = jnp.dot(earlier, onehot.astype(jnp.bfloat16), preferred_element_type=jnp.float32)
    slot = jnp.sum(jnp.where(onehot, counts, 0.0), axis=1).astype(jnp.int32)
    target = flat * capacity + slot
    placing = (target[:, None] == jnp.arange(experts * capacity, dtype=jnp.int32)[None, :]).astype(
        jnp.float32
    )
    picker = jnp.sum(placing.reshape(count, top, experts * capacity), axis=1)
    return (target, placing, picker)


def expert_terms(all_x, all_u, rows_p, block_in, block_out, quarters):
    halves, rows, half = all_x.shape
    ff = block_in.shape[1]
    w_in_h = block_in.reshape(halves, half, ff)
    w_out_h = block_out.reshape(ff, halves, half)
    hidden = jnp.einsum("hrk,hkf->rf", all_x, w_in_h, preferred_element_type=jnp.float32)
    act = jax.nn.silu(hidden).astype(jnp.bfloat16)
    output = jnp.einsum("rf,fhk->hrk", act, w_out_h, preferred_element_type=jnp.float32)
    score = jnp.sum(output * all_u.astype(jnp.float32), axis=(0, 2))
    scaled = (rows_p.astype(jnp.float32)[None, :, None] * all_u.astype(jnp.float32)).astype(
        jnp.bfloat16
    )
    back = jnp.einsum("hrk,fhk->rf", scaled, w_out_h, preferred_element_type=jnp.float32)
    sigma = jax.nn.sigmoid(hidden)
    inner = (sigma * (1.0 + hidden * (1.0 - sigma)) * back).astype(jnp.bfloat16)
    grad_out = jnp.einsum("rf,hrk->fhk", act, scaled, preferred_element_type=jnp.float32)
    grad_in = jnp.einsum("hrk,rf->hkf", all_x, inner, preferred_element_type=jnp.float32)
    w_in_q = block_in.reshape(quarters, halves * half // quarters, ff)
    row_grad = jnp.einsum("rf,qkf->qrk", inner, w_in_q, preferred_element_type=jnp.float32)
    return (
        row_grad,
        score,
        grad_in.reshape(halves * half, ff),
        grad_out.reshape(ff, halves * half),
    )


def per_device(tokens, cotangent, probs, expert_ids, w_in, w_out):
    count, top = expert_ids.shape
    width = tokens.shape[1]
    n_z = lax.axis_size("zlo")
    n_c = lax.axis_size("core")
    part = width // (n_z * n_c)
    d = lax.axis_index("zlo") * n_c + lax.axis_index("core")
    experts = lax.axis_size("expert") * w_in.shape[0]
    capacity = min(count, max(2, (9 * top * count + 8 * experts - 1) // (8 * experts)))
    block_in = w_in[0]
    block_out = w_out[0]
    target, placing, picker = slot_tables(expert_ids, capacity, experts)
    pick = picker.astype(jnp.bfloat16)
    c = lax.axis_index("core")
    half = width // n_c
    x_half = lax.dynamic_slice_in_dim(tokens, c * half, half, axis=1)
    u_half = lax.dynamic_slice_in_dim(cotangent, c * half, half, axis=1)
    xu = jnp.concatenate([x_half, u_half], axis=1)
    slot_xu = lax.dot_general(
        pick, xu, (((0,), (0,)), ((), ())), preferred_element_type=jnp.float32
    ).astype(jnp.bfloat16)
    slot_p = jnp.dot(
        probs.reshape(-1).astype(jnp.float32), placing, precision=lax.Precision.HIGHEST
    ).astype(jnp.bfloat16)
    body = capacity * 2 * half // 128
    packed = jnp.concatenate(
        [
            slot_xu.reshape(experts, body, 128),
            jnp.pad(slot_p.reshape(experts, 1, capacity), ((0, 0), (0, 0), (0, 128 - capacity))),
        ],
        axis=1,
    )
    recv = lax.all_to_all(packed, "expert", split_axis=0, concat_axis=0, tiled=True)
    rows = experts * capacity
    recv_xu = recv[:, :body, :].reshape(rows, 2 * half)
    recv_p = recv[:, body, :capacity].reshape(rows)
    all_xu = lax.all_gather(recv_xu, "core", axis=0, tiled=False)
    all_x = all_xu[..., :half]
    all_u = all_xu[..., half:]
    row_grad, score, grad_in, grad_out = expert_terms(
        all_x, all_u, recv_p, block_in, block_out, n_z * n_c
    )
    rg = row_grad.astype(jnp.bfloat16).reshape(n_z, n_c, rows, part)
    nrow = -(-rows // (16 * part)) * 16
    srow = jnp.pad(score.astype(jnp.bfloat16), (0, nrow * part - rows)).reshape(1, 1, nrow, part)
    chunk = jnp.concatenate([rg, jnp.broadcast_to(srow, (n_z, n_c, nrow, part))], axis=2)
    on_chip = lax.all_to_all(chunk, "core", split_axis=1, concat_axis=1, tiled=True)
    chip_sum = jnp.sum(on_chip[:, :, :rows].astype(jnp.float32), axis=1).astype(jnp.bfloat16)
    chip_scores = on_chip[:, :, rows:].reshape(n_z, n_c * nrow, part)
    chunk2 = jnp.concatenate([chip_sum, chip_scores], axis=1)
    off_chip = lax.all_to_all(chunk2, "zlo", split_axis=0, concat_axis=0, tiled=True)
    row_sum = jnp.sum(off_chip[:, :rows].astype(jnp.float32), axis=0).astype(jnp.bfloat16)
    block_scores = off_chip[:, rows:].reshape(n_z * n_c, nrow * part)[:, :rows]
    score_sum = jnp.sum(block_scores.astype(jnp.float32), axis=0)
    body2 = capacity * part // 128
    packed2 = jnp.concatenate(
        [
            row_sum.reshape(experts, body2, 128),
            jnp.pad(
                score_sum.astype(jnp.bfloat16).reshape(experts, 1, capacity),
                ((0, 0), (0, 0), (0, 128 - capacity)),
            ),
        ],
        axis=1,
    )
    back = lax.all_to_all(packed2, "expert", split_axis=0, concat_axis=0, tiled=True)
    back_x = back[:, :body2, :]
    back_s = back[:, body2, :capacity]
    token_part = jnp.dot(
        pick, back_x.reshape(experts * capacity, part), preferred_element_type=jnp.float32
    )
    grad_tokens = lax.all_gather(token_part.astype(jnp.bfloat16), DP, axis=1, tiled=True)
    gate_grad = (
        jnp.dot(
            placing.astype(jnp.bfloat16), back_s.reshape(-1), preferred_element_type=jnp.float32
        ).reshape(count, top)
    ).astype(jnp.bfloat16)
    grad_w_in = grad_in.astype(jnp.bfloat16)[None]
    grad_w_out = grad_out.astype(jnp.bfloat16)[None]
    return (grad_tokens, gate_grad, grad_w_in, grad_w_out)


def solution(mesh):
    n_dp, n_ex = mesh.devices.shape
    split = Mesh(mesh.devices.reshape(2, n_dp // 2, n_ex), ("zlo", "core", "expert"))
    in_specs = (
        P("expert", None),
        P("expert", None),
        P("expert", None),
        P("expert", None),
        P("expert", None, DP),
        P("expert", DP, None),
    )
    out_specs = (
        P("expert", None),
        P("expert", None),
        P("expert", None, DP),
        P("expert", DP, None),
    )
    return jax.shard_map(
        per_device, mesh=split, in_specs=in_specs, out_specs=out_specs, check_vma=False
    )
```
